32 devices in a mesh: grp: 2 (over x), row: 16 (over z, y, core).
Axes of the slice: x: 2, y: 2, z: 4, core: 2. Of those that a mesh axis runs over, the one named last changes fastest.
Arguments:
- panels: bfloat16 [3, 8192, 1536], P(None, 'row'), may hold values from -0.099436891 to 0.099436891, as said below
- first_f: bfloat16 [1536, 512], P('row', 'grp'), parts along dimension 1, may hold values from -6 to 6
- first_g: bfloat16 [1536, 512], P('row', 'grp'), parts along dimension 1, may hold values from -6 to 6
- phase: float32 [4, 1536], P('grp'), parts along dimension 0, may hold values from -3.140625 to 3.140625
- wavenum: float32 [4, 1536], P('grp'), parts along dimension 0, may hold values from 0.5 to 2
Outputs:
- final_f: float32 [1536, 512], P('row', 'grp'), parts along dimension 1
- final_g: float32 [1536, 512], P('row', 'grp'), parts along dimension 1
The draws below stay inside these ranges and needn't reach their ends.
There are 2 independent parts, one for each index of `grp`. The reference program is written for one: setup_inputs(seed, part) draws one part's arguments, and reference() takes and returns one part's arrays. A program takes and returns all parts, laid end to end along the dimension named above; an argument that names none is the same for every part. Nothing has to cross between parts.
Inputs may be any that keep to these rules, and one draw needn't show every extreme that they name: `panels`: consecutive sectors' surface functions share part of their shape.
All inputs are finite; a program needn't handle non-finite values.
Results may differ from the reference program's by a relative error of at most 0.013.
Values may be sent and summed in bfloat16 or wider, within the bound.
No kernel may reach another device: no remote copies, remote signals or barrier semaphores. Data moves between devices by JAX's collectives and lax.ppermute only.
A program may use at most 64 MiB of HBM per device.

```python
import math
import jax
import jax.numpy as jnp
from jax import lax

POINTS = 8192
CHANNELS = 1536
SOLUTIONS = 256
SECTORS = 2


def draw_panels(key, part):
    base_key, noise_key = jax.random.split(jax.random.fold_in(key, 17))
    base = jnp.clip(jax.random.normal(base_key, (POINTS, CHANNELS), jnp.float32), -6.0, 6.0)
    noise = jnp.clip(jax.random.normal(noise_key, (SECTORS + 1, POINTS, CHANNELS), jnp.float32), -6.0, 6.0)
    mixed = (0.7071 * base[None, :, :] + 0.7071 * noise) / jnp.sqrt(jnp.float32(POINTS))
    return mixed.astype(jnp.bfloat16)


def levels(own_key, extent, cuts, low, top_value):
    gain = 1.0
    for dim, blocks in cuts:
        heights = jax.random.uniform(jax.random.fold_in(jax.random.fold_in(own_key, 6), dim), (blocks,), jnp.float32, low / len(cuts), top_value / len(cuts))
        gain = gain * jnp.repeat(jnp.exp(heights), extent[dim] // blocks).reshape((-1,) + (1,) * (len(extent) - 1 - dim))
    return gain


def centred(key, shape, spread, bound, shards=(), dtype=jnp.bfloat16):
    result = spread * jax.random.normal(key, shape, jnp.float32)
    if shards:
        result = result * levels(key, shape, shards, -0.22, 0.18)
    return jnp.clip(result, -bound, bound).astype(dtype)


def setup_inputs(seed: int = 0, part: int = 0) -> dict:
    splits = jax.random.split(jax.random.key(seed), 6)
    part_splits = jax.random.split(jax.random.fold_in(splits[5], part), 6)
    return {
        "panels": draw_panels(jax.random.fold_in(splits[5], 71), part),
        "first_f": centred(part_splits[1], (CHANNELS, SOLUTIONS), 1.0, 6.0, ((0, 16),)),
        "first_g": centred(part_splits[2], (CHANNELS, SOLUTIONS), 1.0, 6.0, ((0, 16),)),
        "phase": jnp.clip(jax.random.uniform(part_splits[3], (SECTORS, CHANNELS), jnp.float32, -3.140625, 3.140625), -3.140625, 3.140625),
        "wavenum": jnp.clip(jnp.exp(jax.random.uniform(part_splits[4], (SECTORS, CHANNELS), jnp.float32, math.log(0.5), math.log(2.0))), 0.5, 2.0),
    }


def reference(panels, first_f, first_g, phase, wavenum):
    amp = first_f.astype(jnp.float32)
    der = first_g.astype(jnp.float32)
    for sector in range(SECTORS):
        margin = jnp.dot(panels[sector].T, panels[sector + 1], preferred_element_type=jnp.float32).astype(jnp.bfloat16)
        rot_amp = jnp.dot(margin.T, amp.astype(jnp.bfloat16), preferred_element_type=jnp.float32)
        rot_der = jnp.dot(margin.T, der.astype(jnp.bfloat16), preferred_element_type=jnp.float32)
        cosine = jnp.cos(phase[sector])[:, None]
        sine = jnp.sin(phase[sector])[:, None]
        wave = wavenum[sector][:, None]
        new_amp = cosine * rot_amp + sine / wave * rot_der
        new_der = -wave * sine * rot_amp + cosine * rot_der
        norm = lax.optimization_barrier(jnp.sum(new_amp * new_amp, axis=0)) + lax.optimization_barrier(jnp.sum(new_der * new_der, axis=0))
        scale = 1.0 / jnp.sqrt(norm / (2.0 * CHANNELS) + 1e-06)
        amp = new_amp * scale[None, :]
        der = new_der * scale[None, :]
    return (amp, der)
```

```python
import jax
import jax.numpy as jnp
from jax import lax
from jax.sharding import PartitionSpec as P

SECTORS = 2


def contract_rows(left, right):
    return lax.dot_general(
        left, right, (((0,), (0,)), ((), ())), preferred_element_type=jnp.float32
    )


def shards(panels, first_f, first_g, phase, wavenum):
    chan_rows = first_f.shape[0]
    width = first_f.shape[1]
    all_channels = chan_rows * lax.axis_size("row")
    first_row = lax.axis_index("row") * chan_rows
    solutions = lax.all_gather(
        jnp.concatenate([first_f, first_g], axis=1), "row", axis=0, tiled=True
    )
    for sector in range(SECTORS):
        projected = jnp.dot(
            panels[sector], solutions, preferred_element_type=jnp.float32
        ).astype(jnp.bfloat16)
        rotated = lax.psum(contract_rows(panels[sector + 1], projected), "row")
        rot_amp = rotated[:, :width]
        rot_der = rotated[:, width:]
        cosine = jnp.cos(phase[sector])[:, None]
        sine = jnp.sin(phase[sector])[:, None]
        wave = wavenum[sector][:, None]
        new_amp = cosine * rot_amp + sine / wave * rot_der
        new_der = -wave * sine * rot_amp + cosine * rot_der
        norm = jnp.sum(new_amp * new_amp, axis=0) + jnp.sum(new_der * new_der, axis=0)
        scale = 1.0 / jnp.sqrt(norm / (2.0 * all_channels) + 1e-06)
        amp = new_amp * scale[None, :]
        der = new_der * scale[None, :]
        solutions = jnp.concatenate([amp, der], axis=1).astype(jnp.bfloat16)
    amp = lax.dynamic_slice_in_dim(amp, first_row, chan_rows, 0)
    der = lax.dynamic_slice_in_dim(der, first_row, chan_rows, 0)
    return (amp, der)


def solution(mesh):
    in_specs = (
        P(None, "row", None),
        P("row", "grp"),
        P("row", "grp"),
        P("grp", None),
        P("grp", None),
    )
    out_specs = (P("row", "grp"), P("row", "grp"))
    return jax.shard_map(shards, mesh=mesh, in_specs=in_specs, out_specs=out_specs, check_vma=False)
```

```python
import jax
import jax.numpy as jnp
from jax import lax
from jax.sharding import PartitionSpec as P

SECTORS = 2


def contract_rows(left, right):
    return lax.dot_general(
        left, right, (((0,), (0,)), ((), ())), preferred_element_type=jnp.float32
    )


def exchange(x, distance, devices):
    return lax.ppermute(x, "row", [(i, i ^ distance) for i in range(devices)])


def halving_reduce_scatter(z, devices):
    bits = devices.bit_length() - 1
    me = lax.axis_index("row")
    cur = z.reshape((2,) * bits + (z.shape[0] // devices, z.shape[1]))
    for bit in range(bits):
        axis = bits - 1 - bit
        mine = (me >> bit) & 1
        keep = lax.dynamic_index_in_dim(cur, mine, axis=axis, keepdims=False)
        send = lax.dynamic_index_in_dim(cur, 1 - mine, axis=axis, keepdims=False)
        cur = keep + exchange(send, 1 << bit, devices)
    return cur


def doubling_all_gather(x, devices):
    bits = devices.bit_length() - 1
    me = lax.axis_index("row")
    cur = x
    for step in range(bits):
        bit = bits - 1 - step
        other = exchange(cur, 1 << bit, devices)
        low = (me >> bit) & 1 == 0
        cur = jnp.stack(
            [jnp.where(low, cur, other), jnp.where(low, other, cur)], axis=step
        )
    return cur.reshape((-1, x.shape[-1]))


def doubling_all_reduce(x, devices):
    bits = devices.bit_length() - 1
    for bit in range(bits):
        x = x + exchange(x, 1 << bit, devices)
    return x


def shards(panels, first_f, first_g, phase, wavenum):
    chan_rows = first_f.shape[0]
    width = first_f.shape[1]
    devices = lax.axis_size("row")
    all_channels = chan_rows * devices
    first_row = lax.axis_index("row") * chan_rows
    solutions = doubling_all_gather(
        jnp.concatenate([first_f, first_g], axis=1), devices
    )
    scale = None
    for sector in range(SECTORS):
        projected = jnp.dot(panels[sector], solutions, preferred_element_type=jnp.float32)
        if scale is not None:
            projected = projected * jnp.concatenate([scale, scale])[None, :]
        rotated = halving_reduce_scatter(
            contract_rows(panels[sector + 1], projected.astype(jnp.bfloat16)), devices
        )
        rot_amp = rotated[:, :width]
        rot_der = rotated[:, width:]
        angle_rows = lax.dynamic_slice_in_dim(phase[sector], first_row, chan_rows, 0)
        wave_rows = lax.dynamic_slice_in_dim(wavenum[sector], first_row, chan_rows, 0)
        cosine = jnp.cos(angle_rows)[:, None]
        sine = jnp.sin(angle_rows)[:, None]
        wave = wave_rows[:, None]
        new_amp = cosine * rot_amp + sine / wave * rot_der
        new_der = -wave * sine * rot_amp + cosine * rot_der
        if sector + 1 < SECTORS:
            solutions = doubling_all_gather(
                jnp.concatenate([new_amp, new_der], axis=1).astype(jnp.bfloat16), devices
            )
            full = solutions.astype(jnp.float32)
            norm = jnp.sum(full[:, :width] * full[:, :width], axis=0) + jnp.sum(
                full[:, width:] * full[:, width:], axis=0
            )
        else:
            local_norm = jnp.sum(new_amp * new_amp, axis=0) + jnp.sum(new_der * new_der, axis=0)
            norm = doubling_all_reduce(local_norm, devices)
        scale = 1.0 / jnp.sqrt(norm / (2.0 * all_channels) + 1e-06)
    return (new_amp * scale[None, :], new_der * scale[None, :])


def solution(mesh):
    in_specs = (
        P(None, "row", None),
        P("row", "grp"),
        P("row", "grp"),
        P("grp", None),
        P("grp", None),
    )
    out_specs = (P("row", "grp"), P("row", "grp"))
    return jax.shard_map(shards, mesh=mesh, in_specs=in_specs, out_specs=out_specs, check_vma=False)
```

```python
import jax
import jax.numpy as jnp
from jax import lax
from jax.sharding import PartitionSpec as P

SECTORS = 2


def contract_rows(left, right):
    return lax.dot_general(
        left, right, (((0,), (0,)), ((), ())), preferred_element_type=jnp.float32
    )


def exchange(x, distance, devices):
    return lax.ppermute(x, "row", [(i, i ^ distance) for i in range(devices)])


def halving_reduce_scatter(z, devices, order):
    bits = devices.bit_length() - 1
    me = lax.axis_index("row")
    cur = z.reshape((2,) * bits + (z.shape[0] // devices, z.shape[1]))
    left = list(range(bits - 1, -1, -1))
    for bit in order:
        axis = left.index(bit)
        left.remove(bit)
        mine = (me >> bit) & 1
        keep = lax.dynamic_index_in_dim(cur, mine, axis=axis, keepdims=False)
        send = lax.dynamic_index_in_dim(cur, 1 - mine, axis=axis, keepdims=False)
        cur = keep + exchange(send, 1 << bit, devices)
    return cur


def doubling_all_gather(x, devices, order):
    me = lax.axis_index("row")
    cur = x
    done = []
    for bit in order:
        other = exchange(cur, 1 << bit, devices)
        low = (me >> bit) & 1 == 0
        axis = sum(1 for b in done if b > bit)
        done.append(bit)
        cur = jnp.stack(
            [jnp.where(low, cur, other), jnp.where(low, other, cur)], axis=axis
        )
    return cur.reshape((-1, x.shape[-1]))


def doubling_all_reduce(x, devices):
    bits = devices.bit_length() - 1
    for bit in range(bits):
        x = x + exchange(x, 1 << bit, devices)
    return x


def stage_orders(devices):
    bits = list(range(devices.bit_length() - 1))
    if len(bits) < 3:
        return bits, bits
    return bits, [bits[0], bits[2], bits[1]] + bits[3:]


def shards(panels, first_f, first_g, phase, wavenum):
    chan_rows = first_f.shape[0]
    width = first_f.shape[1]
    devices = lax.axis_size("row")
    all_channels = chan_rows * devices
    first_row = lax.axis_index("row") * chan_rows
    order_amp, order_der = stage_orders(devices)
    amp_full = doubling_all_gather(first_f, devices, order_amp[::-1])
    der_full = doubling_all_gather(first_g, devices, order_der[::-1])
    scale = None
    for sector in range(SECTORS):
        solutions = jnp.concatenate([amp_full, der_full], axis=1)
        projected = jnp.dot(panels[sector], solutions, preferred_element_type=jnp.float32)
        if scale is not None:
            projected = projected * jnp.concatenate([scale, scale])[None, :]
        partial = contract_rows(panels[sector + 1], projected.astype(jnp.bfloat16))
        rot_amp = halving_reduce_scatter(partial[:, :width], devices, order_amp)
        rot_der = halving_reduce_scatter(partial[:, width:], devices, order_der)
        angle_rows = lax.dynamic_slice_in_dim(phase[sector], first_row, chan_rows, 0)
        wave_rows = lax.dynamic_slice_in_dim(wavenum[sector], first_row, chan_rows, 0)
        cosine = jnp.cos(angle_rows)[:, None]
        sine = jnp.sin(angle_rows)[:, None]
        wave = wave_rows[:, None]
        new_amp = cosine * rot_amp + sine / wave * rot_der
        new_der = -wave * sine * rot_amp + cosine * rot_der
        if sector + 1 < SECTORS:
            amp_full = doubling_all_gather(new_amp.astype(jnp.bfloat16), devices, order_amp[::-1])
            der_full = doubling_all_gather(new_der.astype(jnp.bfloat16), devices, order_der[::-1])
            amp_wide = amp_full.astype(jnp.float32)
            der_wide = der_full.astype(jnp.float32)
            norm = jnp.sum(amp_wide * amp_wide, axis=0) + jnp.sum(der_wide * der_wide, axis=0)
        else:
            local_norm = jnp.sum(new_amp * new_amp, axis=0) + jnp.sum(new_der * new_der, axis=0)
            norm = doubling_all_reduce(local_norm, devices)
        scale = 1.0 / jnp.sqrt(norm / (2.0 * all_channels) + 1e-06)
    return (new_amp * scale[None, :], new_der * scale[None, :])


def solution(mesh):
    in_specs = (
        P(None, "row", None),
        P("row", "grp"),
        P("row", "grp"),
        P("grp", None),
        P("grp", None),
    )
    out_specs = (P("row", "grp"), P("row", "grp"))
    return jax.shard_map(shards, mesh=mesh, in_specs=in_specs, out_specs=out_specs, check_vma=False)
```

```python
import jax
import jax.numpy as jnp
from jax import lax
from jax.sharding import PartitionSpec as P

SECTORS = 2


def contract_rows(left, right):
    return lax.dot_general(
        left, right, (((0,), (0,)), ((), ())), preferred_element_type=jnp.float32
    )


def exchange(x, distance, devices):
    return lax.ppermute(x, "row", [(i, i ^ distance) for i in range(devices)])


def halving_reduce_scatter(z, devices, order):
    bits = devices.bit_length() - 1
    me = lax.axis_index("row")
    cur = z.reshape((2,) * bits + (z.shape[0] // devices, z.shape[1]))
    left = list(range(bits - 1, -1, -1))
    for bit in order:
        axis = left.index(bit)
        left.remove(bit)
        mine = (me >> bit) & 1
        keep = lax.dynamic_index_in_dim(cur, mine, axis=axis, keepdims=False)
        send = lax.dynamic_index_in_dim(cur, 1 - mine, axis=axis, keepdims=False)
        cur = keep + exchange(send, 1 << bit, devices)
    return cur


def doubling_all_gather(x, devices, order):
    me = lax.axis_index("row")
    cur = x
    done = []
    for bit in order:
        other = exchange(cur, 1 << bit, devices)
        low = (me >> bit) & 1 == 0
        axis = sum(1 for b in done if b > bit)
        done.append(bit)
        cur = jnp.stack(
            [jnp.where(low, cur, other), jnp.where(low, other, cur)], axis=axis
        )
    return cur.reshape((-1, x.shape[-1]))


def doubling_all_reduce(x, devices):
    bits = devices.bit_length() - 1
    for bit in range(bits):
        x = x + exchange(x, 1 << bit, devices)
    return x


def stage_orders(devices):
    bits = list(range(devices.bit_length() - 1))
    if len(bits) < 3:
        return bits, bits
    return bits, [bits[0], bits[2], bits[1]] + bits[3:]


def shards(panels, first_f, first_g, phase, wavenum):
    chan_rows = first_f.shape[0]
    width = first_f.shape[1]
    devices = lax.axis_size("row")
    all_channels = chan_rows * devices
    first_row = lax.axis_index("row") * chan_rows
    order_amp, order_der = stage_orders(devices)
    amp_full = doubling_all_gather(first_f, devices, order_amp[::-1])
    der_full = doubling_all_gather(first_g, devices, order_der[::-1])
    scale = None
    for sector in range(SECTORS):
        halves = []
        for gathered in (amp_full, der_full):
            projected = jnp.dot(panels[sector], gathered, preferred_element_type=jnp.float32)
            if scale is not None:
                projected = projected * scale[None, :]
            halves.append(contract_rows(panels[sector + 1], projected.astype(jnp.bfloat16)))
        rot_amp = halving_reduce_scatter(halves[0], devices, order_amp)
        rot_der = halving_reduce_scatter(halves[1], devices, order_der)
        angle_rows = lax.dynamic_slice_in_dim(phase[sector], first_row, chan_rows, 0)
        wave_rows = lax.dynamic_slice_in_dim(wavenum[sector], first_row, chan_rows, 0)
        cosine = jnp.cos(angle_rows)[:, None]
        sine = jnp.sin(angle_rows)[:, None]
        wave = wave_rows[:, None]
        new_amp = cosine * rot_amp + sine / wave * rot_der
        new_der = -wave * sine * rot_amp + cosine * rot_der
        if sector + 1 < SECTORS:
            amp_full = doubling_all_gather(new_amp.astype(jnp.bfloat16), devices, order_amp[::-1])
            der_full = doubling_all_gather(new_der.astype(jnp.bfloat16), devices, order_der[::-1])
            amp_wide = amp_full.astype(jnp.float32)
            der_wide = der_full.astype(jnp.float32)
            norm = jnp.sum(amp_wide * amp_wide, axis=0) + jnp.sum(der_wide * der_wide, axis=0)
        else:
            local_norm = jnp.sum(new_amp * new_amp, axis=0) + jnp.sum(new_der * new_der, axis=0)
            norm = doubling_all_reduce(local_norm, devices)
        scale = 1.0 / jnp.sqrt(norm / (2.0 * all_channels) + 1e-06)
    return (new_amp * scale[None, :], new_der * scale[None, :])


def solution(mesh):
    in_specs = (
        P(None, "row", None),
        P("row", "grp"),
        P("row", "grp"),
        P("grp", None),
        P("grp", None),
    )
    out_specs = (P("row", "grp"), P("row", "grp"))
    return jax.shard_map(shards, mesh=mesh, in_specs=in_specs, out_specs=out_specs, check_vma=False)
```

```python
import jax
import jax.numpy as jnp
from jax import lax
from jax.sharding import PartitionSpec as P

SECTORS = 2


def contract_rows(left, right):
    return lax.dot_general(
        left, right, (((0,), (0,)), ((), ())), preferred_element_type=jnp.float32
    )


def exchange(x, distance, devices):
    return lax.ppermute(x, "row", [(i, i ^ distance) for i in range(devices)])


def halving_reduce_scatter(z, devices, order):
    bits = devices.bit_length() - 1
    me = lax.axis_index("row")
    cur = z.reshape((2,) * bits + (z.shape[0] // devices, z.shape[1]))
    left = list(range(bits - 1, -1, -1))
    for bit in order:
        axis = left.index(bit)
        left.remove(bit)
        mine = (me >> bit) & 1
        keep = lax.dynamic_index_in_dim(cur, mine, axis=axis, keepdims=False)
        send = lax.dynamic_index_in_dim(cur, 1 - mine, axis=axis, keepdims=False)
        cur = keep + exchange(send, 1 << bit, devices)
    return cur


def doubling_all_gather(x, devices, order):
    me = lax.axis_index("row")
    cur = x
    done = []
    for bit in order:
        other = exchange(cur, 1 << bit, devices)
        low = (me >> bit) & 1 == 0
        axis = sum(1 for b in done if b > bit)
        done.append(bit)
        cur = jnp.stack(
            [jnp.where(low, cur, other), jnp.where(low, other, cur)], axis=axis
        )
    return cur.reshape((-1, x.shape[-1]))


def doubling_all_reduce(x, devices):
    if devices <= 16:
        total = x
        for shift in range(1, devices):
            total = total + exchange(x, shift, devices)
        return total
    bits = devices.bit_length() - 1
    for bit in range(bits):
        x = x + exchange(x, 1 << bit, devices)
    return x


def stage_orders(devices):
    bits = list(range(devices.bit_length() - 1))
    if len(bits) < 3:
        return bits, bits
    return bits, [bits[0], bits[2], bits[1]] + bits[3:]


def shards(panels, first_f, first_g, phase, wavenum):
    chan_rows = first_f.shape[0]
    width = first_f.shape[1]
    devices = lax.axis_size("row")
    all_channels = chan_rows * devices
    first_row = lax.axis_index("row") * chan_rows
    order_amp, order_der = stage_orders(devices)
    amp_full = doubling_all_gather(first_f, devices, order_amp[::-1])
    der_full = doubling_all_gather(first_g, devices, order_der[::-1])
    scale = None
    for sector in range(SECTORS):
        halves = []
        for gathered in (amp_full, der_full):
            projected = jnp.dot(panels[sector], gathered, preferred_element_type=jnp.float32)
            if scale is not None:
                projected = projected * scale[None, :]
            halves.append(contract_rows(panels[sector + 1], projected.astype(jnp.bfloat16)))
        rot_amp = halving_reduce_scatter(halves[0], devices, order_amp)
        rot_der = halving_reduce_scatter(halves[1], devices, order_der)
        angle_rows = lax.dynamic_slice_in_dim(phase[sector], first_row, chan_rows, 0)
        wave_rows = lax.dynamic_slice_in_dim(wavenum[sector], first_row, chan_rows, 0)
        cosine = jnp.cos(angle_rows)[:, None]
        sine = jnp.sin(angle_rows)[:, None]
        wave = wave_rows[:, None]
        new_amp = cosine * rot_amp + sine / wave * rot_der
        new_der = -wave * sine * rot_amp + cosine * rot_der
        if sector + 1 < SECTORS:
            amp_full = doubling_all_gather(new_amp.astype(jnp.bfloat16), devices, order_amp[::-1])
            der_full = doubling_all_gather(new_der.astype(jnp.bfloat16), devices, order_der[::-1])
            amp_wide = amp_full.astype(jnp.float32)
            der_wide = der_full.astype(jnp.float32)
            norm = jnp.sum(amp_wide * amp_wide, axis=0) + jnp.sum(der_wide * der_wide, axis=0)
        else:
            local_norm = jnp.sum(new_amp * new_amp, axis=0) + jnp.sum(new_der * new_der, axis=0)
            norm = doubling_all_reduce(local_norm, devices)
        scale = 1.0 / jnp.sqrt(norm / (2.0 * all_channels) + 1e-06)
    return (new_amp * scale[None, :], new_der * scale[None, :])


def solution(mesh):
    in_specs = (
        P(None, "row", None),
        P("row", "grp"),
        P("row", "grp"),
        P("grp", None),
        P("grp", None),
    )
    out_specs = (P("row", "grp"), P("row", "grp"))
    return jax.shard_map(shards, mesh=mesh, in_specs=in_specs, out_specs=out_specs, check_vma=False)
```

```python
import jax
import jax.numpy as jnp
from jax import lax
from jax.sharding import PartitionSpec as P

SECTORS = 2


def contract_rows(left, right):
    return lax.dot_general(
        left, right, (((0,), (0,)), ((), ())), preferred_element_type=jnp.float32
    )


def exchange(x, distance, devices):
    return lax.ppermute(x, "row", [(i, i ^ distance) for i in range(devices)])


def halving_reduce_scatter(z, devices, order):
    bits = devices.bit_length() - 1
    me = lax.axis_index("row")
    cur = z.reshape((2,) * bits + (z.shape[0] // devices, z.shape[1]))
    left = list(range(bits - 1, -1, -1))
    for bit in order:
        axis = left.index(bit)
        left.remove(bit)
        mine = (me >> bit) & 1
        keep = lax.dynamic_index_in_dim(cur, mine, axis=axis, keepdims=False)
        send = lax.dynamic_index_in_dim(cur, 1 - mine, axis=axis, keepdims=False)
        if bit == 0:
            cur = keep + exchange(send, 1 << bit, devices)
        else:
            cur = keep + exchange(send.astype(jnp.bfloat16), 1 << bit, devices).astype(jnp.float32)
    return cur


def doubling_all_gather(x, devices, order):
    me = lax.axis_index("row")
    cur = x
    done = []
    for bit in order:
        other = exchange(cur, 1 << bit, devices)
        low = (me >> bit) & 1 == 0
        axis = sum(1 for b in done if b > bit)
        done.append(bit)
        cur = jnp.stack(
            [jnp.where(low, cur, other), jnp.where(low, other, cur)], axis=axis
        )
    return cur.reshape((-1, x.shape[-1]))


def doubling_all_reduce(x, devices):
    bits = devices.bit_length() - 1
    for bit in range(bits):
        x = x + exchange(x, 1 << bit, devices)
    return x


def stage_orders(devices):
    bits = list(range(devices.bit_length() - 1))
    if len(bits) < 3:
        return bits, bits
    return bits, [bits[0], bits[2], bits[1]] + bits[3:]


def shards(panels, first_f, first_g, phase, wavenum):
    chan_rows = first_f.shape[0]
    width = first_f.shape[1]
    devices = lax.axis_size("row")
    all_channels = chan_rows * devices
    first_row = lax.axis_index("row") * chan_rows
    order_amp, order_der = stage_orders(devices)
    amp_full = doubling_all_gather(first_f, devices, order_amp[::-1])
    der_full = doubling_all_gather(first_g, devices, order_der[::-1])
    scale = None
    for sector in range(SECTORS):
        halves = []
        for gathered in (amp_full, der_full):
            projected = jnp.dot(panels[sector], gathered, preferred_element_type=jnp.float32)
            if scale is not None:
                projected = projected * scale[None, :]
            halves.append(contract_rows(panels[sector + 1], projected.astype(jnp.bfloat16)))
        rot_amp = halving_reduce_scatter(halves[0], devices, order_amp)
        rot_der = halving_reduce_scatter(halves[1], devices, order_der)
        angle_rows = lax.dynamic_slice_in_dim(phase[sector], first_row, chan_rows, 0)
        wave_rows = lax.dynamic_slice_in_dim(wavenum[sector], first_row, chan_rows, 0)
        cosine = jnp.cos(angle_rows)[:, None]
        sine = jnp.sin(angle_rows)[:, None]
        wave = wave_rows[:, None]
        new_amp = cosine * rot_amp + sine / wave * rot_der
        new_der = -wave * sine * rot_amp + cosine * rot_der
        if sector + 1 < SECTORS:
            amp_full = doubling_all_gather(new_amp.astype(jnp.bfloat16), devices, order_amp[::-1])
            der_full = doubling_all_gather(new_der.astype(jnp.bfloat16), devices, order_der[::-1])
            amp_wide = amp_full.astype(jnp.float32)
            der_wide = der_full.astype(jnp.float32)
            norm = jnp.sum(amp_wide * amp_wide, axis=0) + jnp.sum(der_wide * der_wide, axis=0)
        else:
            local_norm = jnp.sum(new_amp * new_amp, axis=0) + jnp.sum(new_der * new_der, axis=0)
            norm = doubling_all_reduce(local_norm, devices)
        scale = 1.0 / jnp.sqrt(norm / (2.0 * all_channels) + 1e-06)
    return (new_amp * scale[None, :], new_der * scale[None, :])


def solution(mesh):
    in_specs = (
        P(None, "row", None),
        P("row", "grp"),
        P("row", "grp"),
        P("grp", None),
        P("grp", None),
    )
    out_specs = (P("row", "grp"), P("row", "grp"))
    return jax.shard_map(shards, mesh=mesh, in_specs=in_specs, out_specs=out_specs, check_vma=False)
```

```python
import functools

import jax
import jax.numpy as jnp
from jax import lax
from jax.experimental import pallas as pl
from jax.experimental.pallas import tpu as pltpu
from jax.sharding import PartitionSpec as P

SECTORS = 2


def rotate_kernel(sector, panels_ref, state_ref, scale_ref, out_ref):
    projected = jnp.dot(panels_ref[sector], state_ref[...], preferred_element_type=jnp.float32)
    projected = (projected * scale_ref[...]).astype(jnp.bfloat16)
    out_ref[...] = lax.dot_general(
        panels_ref[sector + 1], projected, (((0,), (0,)), ((), ())),
        preferred_element_type=jnp.float32,
    )


def rotate_local(panels, state, scale, sector):
    points, channels = panels.shape[1], panels.shape[2]
    width = state.shape[1]
    vmem = pl.BlockSpec(memory_space=pltpu.VMEM)
    return pl.pallas_call(
        functools.partial(rotate_kernel, sector),
        out_shape=jax.ShapeDtypeStruct((channels, width), jnp.float32),
        in_specs=[vmem, vmem, vmem],
        out_specs=vmem,
        cost_estimate=pl.CostEstimate(
            flops=4 * points * channels * width,
            transcendentals=0,
            bytes_accessed=2 * (panels.size + state.size) + 4 * channels * width,
        ),
    )(panels, state, scale[None, :])


def exchange(x, distance, devices):
    return lax.ppermute(x, "row", [(i, i ^ distance) for i in range(devices)])


def halving_reduce_scatter(z, devices, order):
    bits = devices.bit_length() - 1
    me = lax.axis_index("row")
    cur = z.reshape((2,) * bits + (z.shape[0] // devices, z.shape[1]))
    left = list(range(bits - 1, -1, -1))
    for bit in order:
        axis = left.index(bit)
        left.remove(bit)
        mine = (me >> bit) & 1
        keep = lax.dynamic_index_in_dim(cur, mine, axis=axis, keepdims=False)
        send = lax.dynamic_index_in_dim(cur, 1 - mine, axis=axis, keepdims=False)
        if bit == 0:
            cur = keep + exchange(send, 1 << bit, devices)
        else:
            cur = keep + exchange(send.astype(jnp.bfloat16), 1 << bit, devices).astype(jnp.float32)
    return cur


def doubling_all_gather(x, devices, order):
    me = lax.axis_index("row")
    cur = x
    done = []
    for bit in order:
        other = exchange(cur, 1 << bit, devices)
        low = (me >> bit) & 1 == 0
        axis = sum(1 for b in done if b > bit)
        done.append(bit)
        cur = jnp.stack(
            [jnp.where(low, cur, other), jnp.where(low, other, cur)], axis=axis
        )
    return cur.reshape((-1, x.shape[-1]))


def doubling_all_reduce(x, devices):
    bits = devices.bit_length() - 1
    for bit in range(bits):
        x = x + exchange(x, 1 << bit, devices)
    return x


def stage_orders(devices):
    bits = list(range(devices.bit_length() - 1))
    if len(bits) < 3:
        return bits, bits
    return bits, [bits[0], bits[2], bits[1]] + bits[3:]


def shards(panels, first_f, first_g, phase, wavenum):
    chan_rows = first_f.shape[0]
    width = first_f.shape[1]
    devices = lax.axis_size("row")
    all_channels = chan_rows * devices
    first_row = lax.axis_index("row") * chan_rows
    order_amp, order_der = stage_orders(devices)
    amp_full = doubling_all_gather(first_f, devices, order_amp[::-1])
    der_full = doubling_all_gather(first_g, devices, order_der[::-1])
    scale = None
    for sector in range(SECTORS):
        if scale is None:
            scale = jnp.ones((width,), jnp.float32)
        halves = [rotate_local(panels, gathered, scale, sector) for gathered in (amp_full, der_full)]
        rot_amp = halving_reduce_scatter(halves[0], devices, order_amp)
        rot_der = halving_reduce_scatter(halves[1], devices, order_der)
        angle_rows = lax.dynamic_slice_in_dim(phase[sector], first_row, chan_rows, 0)
        wave_rows = lax.dynamic_slice_in_dim(wavenum[sector], first_row, chan_rows, 0)
        cosine = jnp.cos(angle_rows)[:, None]
        sine = jnp.sin(angle_rows)[:, None]
        wave = wave_rows[:, None]
        new_amp = cosine * rot_amp + sine / wave * rot_der
        new_der = -wave * sine * rot_amp + cosine * rot_der
        if sector + 1 < SECTORS:
            amp_full = doubling_all_gather(new_amp.astype(jnp.bfloat16), devices, order_amp[::-1])
            der_full = doubling_all_gather(new_der.astype(jnp.bfloat16), devices, order_der[::-1])
            amp_wide = amp_full.astype(jnp.float32)
            der_wide = der_full.astype(jnp.float32)
            norm = jnp.sum(amp_wide * amp_wide, axis=0) + jnp.sum(der_wide * der_wide, axis=0)
        else:
            local_norm = jnp.sum(new_amp * new_amp, axis=0) + jnp.sum(new_der * new_der, axis=0)
            norm = doubling_all_reduce(local_norm, devices)
        scale = 1.0 / jnp.sqrt(norm / (2.0 * all_channels) + 1e-06)
    return (new_amp * scale[None, :], new_der * scale[None, :])


def solution(mesh):
    in_specs = (
        P(None, "row", None),
        P("row", "grp"),
        P("row", "grp"),
        P("grp", None),
        P("grp", None),
    )
    out_specs = (P("row", "grp"), P("row", "grp"))
    return jax.shard_map(shards, mesh=mesh, in_specs=in_specs, out_specs=out_specs, check_vma=False)
```

```python
import jax
import jax.numpy as jnp
from jax import lax
from jax.sharding import PartitionSpec as P

SECTORS = 2


def contract_rows(left, right):
    return lax.dot_general(
        left, right, (((0,), (0,)), ((), ())), preferred_element_type=jnp.float32
    )


def exchange(x, distance, devices):
    return lax.ppermute(x, "row", [(i, i ^ distance) for i in range(devices)])


def halving_reduce_scatter(parts, devices, orders):
    bits = devices.bit_length() - 1
    me = lax.axis_index("row")
    curs = [z.reshape((2,) * bits + (z.shape[0] // devices, z.shape[1])) for z in parts]
    lefts = [list(range(bits - 1, -1, -1)) for _ in parts]
    for step in range(bits):
        keeps, sends = [], []
        for i, cur in enumerate(curs):
            bit = orders[i][step]
            axis = lefts[i].index(bit)
            lefts[i].remove(bit)
            mine = (me >> bit) & 1
            keeps.append(lax.dynamic_index_in_dim(cur, mine, axis=axis, keepdims=False))
            send = lax.dynamic_index_in_dim(cur, 1 - mine, axis=axis, keepdims=False)
            if bit != 0:
                send = send.astype(jnp.bfloat16)
            sends.append(send)
        received = grouped_exchange(sends, [order[step] for order in orders], devices)
        curs = [keep + got.astype(jnp.float32) for keep, got in zip(keeps, received)]
    return curs


def grouped_exchange(sends, bits, devices):
    received = [None] * len(sends)
    for bit in sorted(set(bits)):
        members = [i for i, b in enumerate(bits) if b == bit]
        if len(members) == 1:
            received[members[0]] = exchange(sends[members[0]], 1 << bit, devices)
        else:
            got = exchange(jnp.stack([sends[i] for i in members]), 1 << bit, devices)
            for j, i in enumerate(members):
                received[i] = got[j]
    return received


def doubling_all_gather(parts, devices, orders):
    me = lax.axis_index("row")
    curs = list(parts)
    dones = [[] for _ in parts]
    for step in range(len(orders[0])):
        bits = [order[step] for order in orders]
        others = grouped_exchange(curs, bits, devices)
        for i, bit in enumerate(bits):
            low = (me >> bit) & 1 == 0
            axis = sum(1 for b in dones[i] if b > bit)
            dones[i].append(bit)
            curs[i] = jnp.stack(
                [jnp.where(low, curs[i], others[i]), jnp.where(low, others[i], curs[i])], axis=axis
            )
    return [cur.reshape((-1, part.shape[-1])) for cur, part in zip(curs, parts)]


def doubling_all_reduce(x, devices):
    bits = devices.bit_length() - 1
    for bit in range(bits):
        x = x + exchange(x, 1 << bit, devices)
    return x


def stage_orders(devices):
    bits = list(range(devices.bit_length() - 1))
    if len(bits) < 3:
        return bits, bits
    return bits, [bits[0], bits[2], bits[1]] + bits[3:]


def shards(panels, first_f, first_g, phase, wavenum):
    chan_rows = first_f.shape[0]
    width = first_f.shape[1]
    devices = lax.axis_size("row")
    all_channels = chan_rows * devices
    first_row = lax.axis_index("row") * chan_rows
    order_amp, order_der = stage_orders(devices)
    gather_orders = [order_amp[::-1], order_der[::-1]]
    amp_full, der_full = doubling_all_gather([first_f, first_g], devices, gather_orders)
    scale = None
    for sector in range(SECTORS):
        halves = []
        for gathered in (amp_full, der_full):
            projected = jnp.dot(panels[sector], gathered, preferred_element_type=jnp.float32)
            if scale is not None:
                projected = projected * scale[None, :]
            halves.append(contract_rows(panels[sector + 1], projected.astype(jnp.bfloat16)))
        rot_amp, rot_der = halving_reduce_scatter(halves, devices, [order_amp, order_der])
        angle_rows = lax.dynamic_slice_in_dim(phase[sector], first_row, chan_rows, 0)
        wave_rows = lax.dynamic_slice_in_dim(wavenum[sector], first_row, chan_rows, 0)
        cosine = jnp.cos(angle_rows)[:, None]
        sine = jnp.sin(angle_rows)[:, None]
        wave = wave_rows[:, None]
        new_amp = cosine * rot_amp + sine / wave * rot_der
        new_der = -wave * sine * rot_amp + cosine * rot_der
        if sector + 1 < SECTORS:
            amp_full, der_full = doubling_all_gather(
                [new_amp.astype(jnp.bfloat16), new_der.astype(jnp.bfloat16)], devices, gather_orders
            )
            amp_wide = amp_full.astype(jnp.float32)
            der_wide = der_full.astype(jnp.float32)
            norm = jnp.sum(amp_wide * amp_wide, axis=0) + jnp.sum(der_wide * der_wide, axis=0)
        else:
            local_norm = jnp.sum(new_amp * new_amp, axis=0) + jnp.sum(new_der * new_der, axis=0)
            norm = doubling_all_reduce(local_norm, devices)
        scale = 1.0 / jnp.sqrt(norm / (2.0 * all_channels) + 1e-06)
    return (new_amp * scale[None, :], new_der * scale[None, :])


def solution(mesh):
    in_specs = (
        P(None, "row", None),
        P("row", "grp"),
        P("row", "grp"),
        P("grp", None),
        P("grp", None),
    )
    out_specs = (P("row", "grp"), P("row", "grp"))
    return jax.shard_map(shards, mesh=mesh, in_specs=in_specs, out_specs=out_specs, check_vma=False)
```

```python
import jax
import jax.numpy as jnp
from jax import lax
from jax.sharding import PartitionSpec as P

SECTORS = 2


def contract_rows(left, right):
    return lax.dot_general(
        left, right, (((0,), (0,)), ((), ())), preferred_element_type=jnp.float32
    )


def exchange(x, distance, devices):
    return lax.ppermute(x, "row", [(i, i ^ distance) for i in range(devices)])


def halving_reduce_scatter(z, devices, order):
    bits = devices.bit_length() - 1
    me = lax.axis_index("row")
    cur = z.reshape((2,) * bits + (z.shape[0] // devices, z.shape[1]))
    left = list(range(bits - 1, -1, -1))
    for bit in order:
        axis = left.index(bit)
        left.remove(bit)
        mine = (me >> bit) & 1
        keep = lax.dynamic_index_in_dim(cur, mine, axis=axis, keepdims=False)
        send = lax.dynamic_index_in_dim(cur, 1 - mine, axis=axis, keepdims=False)
        cur = keep + exchange(send.astype(jnp.bfloat16), 1 << bit, devices).astype(jnp.float32)
    return cur


def doubling_all_gather(x, devices, order):
    me = lax.axis_index("row")
    cur = x
    done = []
    for bit in order:
        other = exchange(cur, 1 << bit, devices)
        low = (me >> bit) & 1 == 0
        axis = sum(1 for b in done if b > bit)
        done.append(bit)
        cur = jnp.stack(
            [jnp.where(low, cur, other), jnp.where(low, other, cur)], axis=axis
        )
    return cur.reshape((-1, x.shape[-1]))


def doubling_all_reduce(x, devices):
    bits = devices.bit_length() - 1
    for bit in range(bits):
        x = x + exchange(x, 1 << bit, devices)
    return x


def stage_orders(devices):
    bits = list(range(devices.bit_length() - 1))
    if len(bits) < 3:
        return bits, bits
    return bits, [bits[0], bits[2], bits[1]] + bits[3:]


def shards(panels, first_f, first_g, phase, wavenum):
    chan_rows = first_f.shape[0]
    width = first_f.shape[1]
    devices = lax.axis_size("row")
    all_channels = chan_rows * devices
    first_row = lax.axis_index("row") * chan_rows
    order_amp, order_der = stage_orders(devices)
    amp_full = doubling_all_gather(first_f, devices, order_amp[::-1])
    der_full = doubling_all_gather(first_g, devices, order_der[::-1])
    scale = None
    for sector in range(SECTORS):
        halves = []
        for gathered in (amp_full, der_full):
            projected = jnp.dot(panels[sector], gathered, preferred_element_type=jnp.float32)
            if scale is not None:
                projected = projected * scale[None, :]
            halves.append(contract_rows(panels[sector + 1], projected.astype(jnp.bfloat16)))
        rot_amp = halving_reduce_scatter(halves[0], devices, order_amp)
        rot_der = halving_reduce_scatter(halves[1], devices, order_der)
        angle_rows = lax.dynamic_slice_in_dim(phase[sector], first_row, chan_rows, 0)
        wave_rows = lax.dynamic_slice_in_dim(wavenum[sector], first_row, chan_rows, 0)
        cosine = jnp.cos(angle_rows)[:, None]
        sine = jnp.sin(angle_rows)[:, None]
        wave = wave_rows[:, None]
        new_amp = cosine * rot_amp + sine / wave * rot_der
        new_der = -wave * sine * rot_amp + cosine * rot_der
        if sector + 1 < SECTORS:
            amp_full = doubling_all_gather(new_amp.astype(jnp.bfloat16), devices, order_amp[::-1])
            der_full = doubling_all_gather(new_der.astype(jnp.bfloat16), devices, order_der[::-1])
            amp_wide = amp_full.astype(jnp.float32)
            der_wide = der_full.astype(jnp.float32)
            norm = jnp.sum(amp_wide * amp_wide, axis=0) + jnp.sum(der_wide * der_wide, axis=0)
        else:
            local_norm = jnp.sum(new_amp * new_amp, axis=0) + jnp.sum(new_der * new_der, axis=0)
            norm = doubling_all_reduce(local_norm, devices)
        scale = 1.0 / jnp.sqrt(norm / (2.0 * all_channels) + 1e-06)
    return (new_amp * scale[None, :], new_der * scale[None, :])


def solution(mesh):
    in_specs = (
        P(None, "row", None),
        P("row", "grp"),
        P("row", "grp"),
        P("grp", None),
        P("grp", None),
    )
    out_specs = (P("row", "grp"), P("row", "grp"))
    return jax.shard_map(shards, mesh=mesh, in_specs=in_specs, out_specs=out_specs, check_vma=False)
```

```python
import jax
import jax.numpy as jnp
from jax import lax
from jax.sharding import PartitionSpec as P

SECTORS = 2


def contract_rows(left, right):
    return lax.dot_general(
        left, right, (((0,), (0,)), ((), ())), preferred_element_type=jnp.float32
    )


def exchange(x, distance, devices):
    return lax.ppermute(x, "row", [(i, i ^ distance) for i in range(devices)])


def halving_reduce_scatter(z, devices, order):
    bits = devices.bit_length() - 1
    me = lax.axis_index("row")
    cur = z.reshape((2,) * bits + (z.shape[0] // devices, z.shape[1]))
    left = list(range(bits - 1, -1, -1))
    for bit in order:
        axis = left.index(bit)
        left.remove(bit)
        mine = (me >> bit) & 1
        keep = lax.dynamic_index_in_dim(cur, mine, axis=axis, keepdims=False)
        send = lax.dynamic_index_in_dim(cur, 1 - mine, axis=axis, keepdims=False)
        cur = keep + exchange(send.astype(jnp.bfloat16), 1 << bit, devices).astype(jnp.float32)
    return cur


def doubling_all_gather(x, devices, order, carry=None):
    me = lax.axis_index("row")
    cur = x
    done = []
    for bit in order:
        other = exchange(cur, 1 << bit, devices)
        if carry is not None:
            other, carry = lax.optimization_barrier((other, carry))
        low = (me >> bit) & 1 == 0
        axis = sum(1 for b in done if b > bit)
        done.append(bit)
        cur = jnp.stack(
            [jnp.where(low, cur, other), jnp.where(low, other, cur)], axis=axis
        )
    result = cur.reshape((-1, x.shape[-1]))
    return result if carry is None else (result, carry)


def doubling_all_reduce(x, devices):
    bits = devices.bit_length() - 1
    for bit in range(bits):
        x = x + exchange(x, 1 << bit, devices)
    return x


def stage_orders(devices):
    bits = list(range(devices.bit_length() - 1))
    if len(bits) < 3:
        return bits, bits
    return bits, [bits[0], bits[2], bits[1]] + bits[3:]


def shards(panels, first_f, first_g, phase, wavenum):
    chan_rows = first_f.shape[0]
    width = first_f.shape[1]
    devices = lax.axis_size("row")
    all_channels = chan_rows * devices
    first_row = lax.axis_index("row") * chan_rows
    order_amp, order_der = stage_orders(devices)
    coefficients = []
    for sector in range(SECTORS):
        angle_rows = lax.dynamic_slice_in_dim(phase[sector], first_row, chan_rows, 0)
        wave_rows = lax.dynamic_slice_in_dim(wavenum[sector], first_row, chan_rows, 0)
        cosine = jnp.cos(angle_rows)[:, None]
        sine = jnp.sin(angle_rows)[:, None]
        wave = wave_rows[:, None]
        coefficients.append((cosine, sine / wave, -wave * sine))
    amp_full, coefficients = doubling_all_gather(
        first_f, devices, order_amp[::-1], carry=coefficients
    )
    der_full = doubling_all_gather(first_g, devices, order_der[::-1])
    scale = None
    for sector in range(SECTORS):
        halves = []
        for gathered in (amp_full, der_full):
            projected = jnp.dot(panels[sector], gathered, preferred_element_type=jnp.float32)
            if scale is not None:
                projected = projected * scale[None, :]
            halves.append(contract_rows(panels[sector + 1], projected.astype(jnp.bfloat16)))
        rot_amp = halving_reduce_scatter(halves[0], devices, order_amp)
        rot_der = halving_reduce_scatter(halves[1], devices, order_der)
        cosine, sine_over_wave, minus_wave_sine = coefficients[sector]
        new_amp = cosine * rot_amp + sine_over_wave * rot_der
        new_der = minus_wave_sine * rot_amp + cosine * rot_der
        if sector + 1 < SECTORS:
            amp_full = doubling_all_gather(new_amp.astype(jnp.bfloat16), devices, order_amp[::-1])
            der_full = doubling_all_gather(new_der.astype(jnp.bfloat16), devices, order_der[::-1])
            amp_wide = amp_full.astype(jnp.float32)
            der_wide = der_full.astype(jnp.float32)
            norm = jnp.sum(amp_wide * amp_wide, axis=0) + jnp.sum(der_wide * der_wide, axis=0)
        else:
            local_norm = jnp.sum(new_amp * new_amp, axis=0) + jnp.sum(new_der * new_der, axis=0)
            norm = doubling_all_reduce(local_norm, devices)
        scale = 1.0 / jnp.sqrt(norm / (2.0 * all_channels) + 1e-06)
    return (new_amp * scale[None, :], new_der * scale[None, :])


def solution(mesh):
    in_specs = (
        P(None, "row", None),
        P("row", "grp"),
        P("row", "grp"),
        P("grp", None),
        P("grp", None),
    )
    out_specs = (P("row", "grp"), P("row", "grp"))
    return jax.shard_map(shards, mesh=mesh, in_specs=in_specs, out_specs=out_specs, check_vma=False)
```

```python
import jax
import jax.numpy as jnp
from jax import lax
from jax.sharding import PartitionSpec as P

SECTORS = 2


def contract_rows(left, right):
    return lax.dot_general(
        left, right, (((0,), (0,)), ((), ())), preferred_element_type=jnp.float32
    )


def exchange(x, distance, devices):
    return lax.ppermute(x, "row", [(i, i ^ distance) for i in range(devices)])


def halving_reduce_scatter(z, devices, order):
    bits = devices.bit_length() - 1
    me = lax.axis_index("row")
    cur = z.reshape((2,) * bits + (z.shape[0] // devices, z.shape[1]))
    left = list(range(bits - 1, -1, -1))
    for bit in order:
        axis = left.index(bit)
        left.remove(bit)
        mine = (me >> bit) & 1
        keep = lax.dynamic_index_in_dim(cur, mine, axis=axis, keepdims=False)
        send = lax.dynamic_index_in_dim(cur, 1 - mine, axis=axis, keepdims=False)
        cur = keep + exchange(send.astype(jnp.bfloat16), 1 << bit, devices).astype(jnp.float32)
    return cur


def doubling_all_gather(x, devices, order):
    me = lax.axis_index("row")
    cur = x
    done = []
    for bit in order:
        other = exchange(cur, 1 << bit, devices)
        low = (me >> bit) & 1 == 0
        axis = sum(1 for b in done if b > bit)
        done.append(bit)
        cur = jnp.stack(
            [jnp.where(low, cur, other), jnp.where(low, other, cur)], axis=axis
        )
    return cur.reshape((-1, x.shape[-1]))


def doubling_all_reduce(x, devices):
    bits = devices.bit_length() - 1
    low = 0
    while low < bits:
        width = 2 if low + 1 < bits else 1
        total = x
        for digit in range(1, 1 << width):
            total = total + exchange(x, digit << low, devices)
        x = total
        low += width
    return x


def stage_orders(devices):
    bits = list(range(devices.bit_length() - 1))
    if len(bits) < 3:
        return bits, bits
    return bits, [bits[0], bits[2], bits[1]] + bits[3:]


def shards(panels, first_f, first_g, phase, wavenum):
    chan_rows = first_f.shape[0]
    width = first_f.shape[1]
    devices = lax.axis_size("row")
    all_channels = chan_rows * devices
    first_row = lax.axis_index("row") * chan_rows
    order_amp, order_der = stage_orders(devices)
    amp_full = doubling_all_gather(first_f, devices, order_amp[::-1])
    der_full = doubling_all_gather(first_g, devices, order_der[::-1])
    scale = None
    for sector in range(SECTORS):
        halves = []
        for gathered in (amp_full, der_full):
            projected = jnp.dot(panels[sector], gathered, preferred_element_type=jnp.float32)
            if scale is not None:
                projected = projected * scale[None, :]
            halves.append(contract_rows(panels[sector + 1], projected.astype(jnp.bfloat16)))
        rot_amp = halving_reduce_scatter(halves[0], devices, order_amp)
        rot_der = halving_reduce_scatter(halves[1], devices, order_der)
        angle_rows = lax.dynamic_slice_in_dim(phase[sector], first_row, chan_rows, 0)
        wave_rows = lax.dynamic_slice_in_dim(wavenum[sector], first_row, chan_rows, 0)
        cosine = jnp.cos(angle_rows)[:, None]
        sine = jnp.sin(angle_rows)[:, None]
        wave = wave_rows[:, None]
        new_amp = cosine * rot_amp + sine / wave * rot_der
        new_der = -wave * sine * rot_amp + cosine * rot_der
        if sector + 1 < SECTORS:
            amp_full = doubling_all_gather(new_amp.astype(jnp.bfloat16), devices, order_amp[::-1])
            der_full = doubling_all_gather(new_der.astype(jnp.bfloat16), devices, order_der[::-1])
            amp_wide = amp_full.astype(jnp.float32)
            der_wide = der_full.astype(jnp.float32)
            norm = jnp.sum(amp_wide * amp_wide, axis=0) + jnp.sum(der_wide * der_wide, axis=0)
        else:
            local_norm = jnp.sum(new_amp * new_amp, axis=0) + jnp.sum(new_der * new_der, axis=0)
            norm = doubling_all_reduce(local_norm, devices)
        scale = 1.0 / jnp.sqrt(norm / (2.0 * all_channels) + 1e-06)
    return (new_amp * scale[None, :], new_der * scale[None, :])


def solution(mesh):
    in_specs = (
        P(None, "row", None),
        P("row", "grp"),
        P("row", "grp"),
        P("grp", None),
        P("grp", None),
    )
    out_specs = (P("row", "grp"), P("row", "grp"))
    return jax.shard_map(shards, mesh=mesh, in_specs=in_specs, out_specs=out_specs, check_vma=False)
```

```python
import jax
import jax.numpy as jnp
from jax import lax
from jax.sharding import PartitionSpec as P

SECTORS = 2


def contract_rows(left, right):
    return lax.dot_general(
        left, right, (((0,), (0,)), ((), ())), preferred_element_type=jnp.float32
    )


def exchange(x, distance, devices):
    return lax.ppermute(x, "row", [(i, i ^ distance) for i in range(devices)])


def halving_reduce_scatter(z, devices, order):
    bits = devices.bit_length() - 1
    me = lax.axis_index("row")
    cur = z.reshape((2,) * bits + (z.shape[0] // devices, z.shape[1]))
    left = list(range(bits - 1, -1, -1))
    for bit in order:
        axis = left.index(bit)
        left.remove(bit)
        mine = (me >> bit) & 1
        keep = lax.dynamic_index_in_dim(cur, mine, axis=axis, keepdims=False)
        send = lax.dynamic_index_in_dim(cur, 1 - mine, axis=axis, keepdims=False)
        cur = keep + exchange(send.astype(jnp.bfloat16), 1 << bit, devices).astype(jnp.float32)
    return cur


def doubling_all_gather(x, devices, order):
    me = lax.axis_index("row")
    cur = x
    axes = []
    for start in range(0, len(order), 2):
        group = order[start:start + 2]
        n = len(group)
        mine = sum(((me >> bit) & 1) << (n - 1 - k) for k, bit in enumerate(group))
        blocks = [cur]
        for digit in range(1, 1 << n):
            xor = sum(((digit >> (n - 1 - k)) & 1) << bit for k, bit in enumerate(group))
            blocks.append(exchange(cur, xor, devices))
        slots = [lax.select_n(slot ^ mine, *blocks) for slot in range(1 << n)]
        lead = len(axes)
        cur = jnp.stack(slots, axis=lead).reshape(
            cur.shape[:lead] + (2,) * n + cur.shape[lead:]
        )
        axes += group
    perm = sorted(range(len(axes)), key=lambda k: -axes[k])
    cur = jnp.transpose(cur, perm + [len(axes), len(axes) + 1])
    return cur.reshape((-1, x.shape[-1]))


def doubling_all_reduce(x, devices):
    bits = devices.bit_length() - 1
    low = 0
    while low < bits:
        width = 2 if low + 1 < bits else 1
        total = x
        for digit in range(1, 1 << width):
            total = total + exchange(x, digit << low, devices)
        x = total
        low += width
    return x


def stage_orders(devices):
    bits = list(range(devices.bit_length() - 1))
    if len(bits) < 3:
        return bits, bits
    return bits, [bits[0], bits[2], bits[1]] + bits[3:]


def shards(panels, first_f, first_g, phase, wavenum):
    chan_rows = first_f.shape[0]
    width = first_f.shape[1]
    devices = lax.axis_size("row")
    all_channels = chan_rows * devices
    first_row = lax.axis_index("row") * chan_rows
    order_amp, order_der = stage_orders(devices)
    amp_full = doubling_all_gather(first_f, devices, order_amp[::-1])
    der_full = doubling_all_gather(first_g, devices, order_der[::-1])
    scale = None
    for sector in range(SECTORS):
        halves = []
        for gathered in (amp_full, der_full):
            projected = jnp.dot(panels[sector], gathered, preferred_element_type=jnp.float32)
            if scale is not None:
                projected = projected * scale[None, :]
            halves.append(contract_rows(panels[sector + 1], projected.astype(jnp.bfloat16)))
        rot_amp = halving_reduce_scatter(halves[0], devices, order_amp)
        rot_der = halving_reduce_scatter(halves[1], devices, order_der)
        angle_rows = lax.dynamic_slice_in_dim(phase[sector], first_row, chan_rows, 0)
        wave_rows = lax.dynamic_slice_in_dim(wavenum[sector], first_row, chan_rows, 0)
        cosine = jnp.cos(angle_rows)[:, None]
        sine = jnp.sin(angle_rows)[:, None]
        wave = wave_rows[:, None]
        new_amp = cosine * rot_amp + sine / wave * rot_der
        new_der = -wave * sine * rot_amp + cosine * rot_der
        if sector + 1 < SECTORS:
            amp_full = doubling_all_gather(new_amp.astype(jnp.bfloat16), devices, order_amp[::-1])
            der_full = doubling_all_gather(new_der.astype(jnp.bfloat16), devices, order_der[::-1])
            amp_wide = amp_full.astype(jnp.float32)
            der_wide = der_full.astype(jnp.float32)
            norm = jnp.sum(amp_wide * amp_wide, axis=0) + jnp.sum(der_wide * der_wide, axis=0)
        else:
            local_norm = jnp.sum(new_amp * new_amp, axis=0) + jnp.sum(new_der * new_der, axis=0)
            norm = doubling_all_reduce(local_norm, devices)
        scale = 1.0 / jnp.sqrt(norm / (2.0 * all_channels) + 1e-06)
    return (new_amp * scale[None, :], new_der * scale[None, :])


def solution(mesh):
    in_specs = (
        P(None, "row", None),
        P("row", "grp"),
        P("row", "grp"),
        P("grp", None),
        P("grp", None),
    )
    out_specs = (P("row", "grp"), P("row", "grp"))
    return jax.shard_map(shards, mesh=mesh, in_specs=in_specs, out_specs=out_specs, check_vma=False)
```

```python
import jax
import jax.numpy as jnp
from jax import lax
from jax.sharding import PartitionSpec as P

SECTORS = 2


def contract_rows(left, right):
    return lax.dot_general(
        left, right, (((0,), (0,)), ((), ())), preferred_element_type=jnp.float32
    )


def exchange(x, distance, devices):
    return lax.ppermute(x, "row", [(i, i ^ distance) for i in range(devices)])


def halving_reduce_scatter(z, devices, order):
    bits = devices.bit_length() - 1
    me = lax.axis_index("row")
    cur = z.reshape((2,) * bits + (z.shape[0] // devices, z.shape[1]))
    left = list(range(bits - 1, -1, -1))
    for bit in order:
        axis = left.index(bit)
        left.remove(bit)
        mine = (me >> bit) & 1
        keep = lax.dynamic_index_in_dim(cur, mine, axis=axis, keepdims=False)
        send = lax.dynamic_index_in_dim(cur, 1 - mine, axis=axis, keepdims=False)
        cur = keep + exchange(send.astype(jnp.bfloat16), 1 << bit, devices).astype(jnp.float32)
    return cur


def doubling_all_gather(parts, devices, orders):
    me = lax.axis_index("row")
    curs = list(parts)
    dones = [[] for _ in parts]
    for step in range(len(orders[0])):
        bits = [order[step] for order in orders]
        others = [None] * len(curs)
        for bit in sorted(set(bits)):
            members = [i for i, b in enumerate(bits) if b == bit]
            if len(members) == 1:
                others[members[0]] = exchange(curs[members[0]], 1 << bit, devices)
            else:
                got = exchange(jnp.stack([curs[i] for i in members]), 1 << bit, devices)
                for j, i in enumerate(members):
                    others[i] = got[j]
        for i, bit in enumerate(bits):
            low = (me >> bit) & 1 == 0
            axis = sum(1 for b in dones[i] if b > bit)
            dones[i].append(bit)
            curs[i] = jnp.stack(
                [jnp.where(low, curs[i], others[i]), jnp.where(low, others[i], curs[i])], axis=axis
            )
    return [cur.reshape((-1, part.shape[-1])) for cur, part in zip(curs, parts)]


def doubling_all_reduce(x, devices):
    bits = devices.bit_length() - 1
    low = 0
    while low < bits:
        width = 2 if low + 1 < bits else 1
        total = x
        for digit in range(1, 1 << width):
            total = total + exchange(x, digit << low, devices)
        x = total
        low += width
    return x


def stage_orders(devices):
    bits = list(range(devices.bit_length() - 1))
    if len(bits) < 3:
        return bits, bits
    return bits, [bits[0], bits[2], bits[1]] + bits[3:]


def shards(panels, first_f, first_g, phase, wavenum):
    chan_rows = first_f.shape[0]
    width = first_f.shape[1]
    devices = lax.axis_size("row")
    all_channels = chan_rows * devices
    first_row = lax.axis_index("row") * chan_rows
    order_amp, order_der = stage_orders(devices)
    gather_orders = [order_amp[::-1], order_der[::-1]]
    amp_full, der_full = doubling_all_gather([first_f, first_g], devices, gather_orders)
    scale = None
    for sector in range(SECTORS):
        halves = []
        for gathered in (amp_full, der_full):
            projected = jnp.dot(panels[sector], gathered, preferred_element_type=jnp.float32)
            if scale is not None:
                projected = projected * scale[None, :]
            halves.append(contract_rows(panels[sector + 1], projected.astype(jnp.bfloat16)))
        rot_amp = halving_reduce_scatter(halves[0], devices, order_amp)
        rot_der = halving_reduce_scatter(halves[1], devices, order_der)
        angle_rows = lax.dynamic_slice_in_dim(phase[sector], first_row, chan_rows, 0)
        wave_rows = lax.dynamic_slice_in_dim(wavenum[sector], first_row, chan_rows, 0)
        cosine = jnp.cos(angle_rows)[:, None]
        sine = jnp.sin(angle_rows)[:, None]
        wave = wave_rows[:, None]
        new_amp = cosine * rot_amp + sine / wave * rot_der
        new_der = -wave * sine * rot_amp + cosine * rot_der
        if sector + 1 < SECTORS:
            amp_full, der_full = doubling_all_gather(
                [new_amp.astype(jnp.bfloat16), new_der.astype(jnp.bfloat16)], devices, gather_orders
            )
            amp_wide = amp_full.astype(jnp.float32)
            der_wide = der_full.astype(jnp.float32)
            norm = jnp.sum(amp_wide * amp_wide, axis=0) + jnp.sum(der_wide * der_wide, axis=0)
        else:
            local_norm = jnp.sum(new_amp * new_amp, axis=0) + jnp.sum(new_der * new_der, axis=0)
            norm = doubling_all_reduce(local_norm, devices)
        scale = 1.0 / jnp.sqrt(norm / (2.0 * all_channels) + 1e-06)
    return (new_amp * scale[None, :], new_der * scale[None, :])


def solution(mesh):
    in_specs = (
        P(None, "row", None),
        P("row", "grp"),
        P("row", "grp"),
        P("grp", None),
        P("grp", None),
    )
    out_specs = (P("row", "grp"), P("row", "grp"))
    return jax.shard_map(shards, mesh=mesh, in_specs=in_specs, out_specs=out_specs, check_vma=False)
```

```python
import jax
import jax.numpy as jnp
from jax import lax
from jax.sharding import PartitionSpec as P

SECTORS = 2


def contract_rows(left, right):
    return lax.dot_general(
        left, right, (((0,), (0,)), ((), ())), preferred_element_type=jnp.float32
    )


def exchange(x, distance, devices):
    return lax.ppermute(x, "row", [(i, i ^ distance) for i in range(devices)])


def halving_reduce_scatter(z, devices, order):
    bits = devices.bit_length() - 1
    me = lax.axis_index("row")
    cur = z.reshape((2,) * bits + (z.shape[0] // devices, z.shape[1]))
    left = list(range(bits - 1, -1, -1))
    for bit in order:
        axis = left.index(bit)
        left.remove(bit)
        mine = (me >> bit) & 1
        keep = lax.dynamic_index_in_dim(cur, mine, axis=axis, keepdims=False)
        send = lax.dynamic_index_in_dim(cur, 1 - mine, axis=axis, keepdims=False)
        cur = keep.astype(jnp.float32) + exchange(
            send.astype(jnp.bfloat16), 1 << bit, devices
        ).astype(jnp.float32)
    return cur


def doubling_all_gather(x, devices, order):
    me = lax.axis_index("row")
    cur = x
    done = []
    for bit in order:
        other = exchange(cur, 1 << bit, devices)
        low = (me >> bit) & 1 == 0
        axis = sum(1 for b in done if b > bit)
        done.append(bit)
        cur = jnp.stack(
            [jnp.where(low, cur, other), jnp.where(low, other, cur)], axis=axis
        )
    return cur.reshape((-1, x.shape[-1]))


def doubling_all_reduce(x, devices):
    bits = devices.bit_length() - 1
    low = 0
    while low < bits:
        width = 2 if low + 1 < bits else 1
        total = x
        for digit in range(1, 1 << width):
            total = total + exchange(x, digit << low, devices)
        x = total
        low += width
    return x


def stage_orders(devices):
    bits = list(range(devices.bit_length() - 1))
    if len(bits) < 3:
        return bits, bits
    return bits, [bits[0], bits[2], bits[1]] + bits[3:]


def shards(panels, first_f, first_g, phase, wavenum):
    chan_rows = first_f.shape[0]
    width = first_f.shape[1]
    devices = lax.axis_size("row")
    all_channels = chan_rows * devices
    first_row = lax.axis_index("row") * chan_rows
    order_amp, order_der = stage_orders(devices)
    amp_full = doubling_all_gather(first_f, devices, order_amp[::-1])
    der_full = doubling_all_gather(first_g, devices, order_der[::-1])
    scale = None
    for sector in range(SECTORS):
        halves = []
        for gathered in (amp_full, der_full):
            projected = jnp.dot(panels[sector], gathered, preferred_element_type=jnp.float32)
            if scale is not None:
                projected = projected * scale[None, :]
            halves.append(
                contract_rows(panels[sector + 1], projected.astype(jnp.bfloat16)).astype(jnp.bfloat16)
            )
        rot_amp = halving_reduce_scatter(halves[0], devices, order_amp)
        rot_der = halving_reduce_scatter(halves[1], devices, order_der)
        angle_rows = lax.dynamic_slice_in_dim(phase[sector], first_row, chan_rows, 0)
        wave_rows = lax.dynamic_slice_in_dim(wavenum[sector], first_row, chan_rows, 0)
        cosine = jnp.cos(angle_rows)[:, None]
        sine = jnp.sin(angle_rows)[:, None]
        wave = wave_rows[:, None]
        new_amp = cosine * rot_amp + sine / wave * rot_der
        new_der = -wave * sine * rot_amp + cosine * rot_der
        if sector + 1 < SECTORS:
            amp_full = doubling_all_gather(new_amp.astype(jnp.bfloat16), devices, order_amp[::-1])
            der_full = doubling_all_gather(new_der.astype(jnp.bfloat16), devices, order_der[::-1])
            amp_wide = amp_full.astype(jnp.float32)
            der_wide = der_full.astype(jnp.float32)
            norm = jnp.sum(amp_wide * amp_wide, axis=0) + jnp.sum(der_wide * der_wide, axis=0)
        else:
            local_norm = jnp.sum(new_amp * new_amp, axis=0) + jnp.sum(new_der * new_der, axis=0)
            norm = doubling_all_reduce(local_norm, devices)
        scale = 1.0 / jnp.sqrt(norm / (2.0 * all_channels) + 1e-06)
    return (new_amp * scale[None, :], new_der * scale[None, :])


def solution(mesh):
    in_specs = (
        P(None, "row", None),
        P("row", "grp"),
        P("row", "grp"),
        P("grp", None),
        P("grp", None),
    )
    out_specs = (P("row", "grp"), P("row", "grp"))
    return jax.shard_map(shards, mesh=mesh, in_specs=in_specs, out_specs=out_specs, check_vma=False)
```

```python
import jax
import jax.numpy as jnp
from jax import lax
from jax.sharding import PartitionSpec as P

SECTORS = 2


def contract_rows(left, right):
    return lax.dot_general(
        left, right, (((0,), (0,)), ((), ())), preferred_element_type=jnp.float32
    )


def exchange(x, distance, devices):
    return lax.ppermute(x, "row", [(i, i ^ distance) for i in range(devices)])


def halving_reduce_scatter(z, devices, order):
    bits = devices.bit_length() - 1
    me = lax.axis_index("row")
    cur = z.reshape((2,) * bits + (z.shape[0] // devices, z.shape[1]))
    left = list(range(bits - 1, -1, -1))
    for bit in order:
        axis = left.index(bit)
        left.remove(bit)
        mine = (me >> bit) & 1
        keep = lax.dynamic_index_in_dim(cur, mine, axis=axis, keepdims=False)
        send = lax.dynamic_index_in_dim(cur, 1 - mine, axis=axis, keepdims=False)
        cur = keep.astype(jnp.float32) + exchange(
            send.astype(jnp.bfloat16), 1 << bit, devices
        ).astype(jnp.float32)
        if bit != order[-1]:
            cur = cur.astype(jnp.bfloat16)
    return cur


def doubling_all_gather(x, devices, order):
    me = lax.axis_index("row")
    cur = x
    done = []
    for bit in order:
        other = exchange(cur, 1 << bit, devices)
        low = (me >> bit) & 1 == 0
        axis = sum(1 for b in done if b > bit)
        done.append(bit)
        cur = jnp.stack(
            [jnp.where(low, cur, other), jnp.where(low, other, cur)], axis=axis
        )
    return cur.reshape((-1, x.shape[-1]))


def doubling_all_reduce(x, devices):
    bits = devices.bit_length() - 1
    low = 0
    while low < bits:
        width = 2 if low + 1 < bits else 1
        total = x
        for digit in range(1, 1 << width):
            total = total + exchange(x, digit << low, devices)
        x = total
        low += width
    return x


def stage_orders(devices):
    bits = list(range(devices.bit_length() - 1))
    if len(bits) < 3:
        return bits, bits
    return bits, [bits[0], bits[2], bits[1]] + bits[3:]


def shards(panels, first_f, first_g, phase, wavenum):
    chan_rows = first_f.shape[0]
    width = first_f.shape[1]
    devices = lax.axis_size("row")
    all_channels = chan_rows * devices
    first_row = lax.axis_index("row") * chan_rows
    order_amp, order_der = stage_orders(devices)
    amp_full = doubling_all_gather(first_f, devices, order_amp[::-1])
    der_full = doubling_all_gather(first_g, devices, order_der[::-1])
    scale = None
    for sector in range(SECTORS):
        halves = []
        for gathered in (amp_full, der_full):
            projected = jnp.dot(panels[sector], gathered, preferred_element_type=jnp.float32)
            if scale is not None:
                projected = projected * scale[None, :]
            halves.append(
                contract_rows(panels[sector + 1], projected.astype(jnp.bfloat16)).astype(jnp.bfloat16)
            )
        rot_amp = halving_reduce_scatter(halves[0], devices, order_amp)
        rot_der = halving_reduce_scatter(halves[1], devices, order_der)
        angle_rows = lax.dynamic_slice_in_dim(phase[sector], first_row, chan_rows, 0)
        wave_rows = lax.dynamic_slice_in_dim(wavenum[sector], first_row, chan_rows, 0)
        cosine = jnp.cos(angle_rows)[:, None]
        sine = jnp.sin(angle_rows)[:, None]
        wave = wave_rows[:, None]
        new_amp = cosine * rot_amp + sine / wave * rot_der
        new_der = -wave * sine * rot_amp + cosine * rot_der
        if sector + 1 < SECTORS:
            amp_full = doubling_all_gather(new_amp.astype(jnp.bfloat16), devices, order_amp[::-1])
            der_full = doubling_all_gather(new_der.astype(jnp.bfloat16), devices, order_der[::-1])
            amp_wide = amp_full.astype(jnp.float32)
            der_wide = der_full.astype(jnp.float32)
            norm = jnp.sum(amp_wide * amp_wide, axis=0) + jnp.sum(der_wide * der_wide, axis=0)
        else:
            local_norm = jnp.sum(new_amp * new_amp, axis=0) + jnp.sum(new_der * new_der, axis=0)
            norm = doubling_all_reduce(local_norm, devices)
        scale = 1.0 / jnp.sqrt(norm / (2.0 * all_channels) + 1e-06)
    return (new_amp * scale[None, :], new_der * scale[None, :])


def solution(mesh):
    in_specs = (
        P(None, "row", None),
        P("row", "grp"),
        P("row", "grp"),
        P("grp", None),
        P("grp", None),
    )
    out_specs = (P("row", "grp"), P("row", "grp"))
    return jax.shard_map(shards, mesh=mesh, in_specs=in_specs, out_specs=out_specs, check_vma=False)
```

```python
import jax
import jax.numpy as jnp
from jax import lax
from jax.sharding import PartitionSpec as P

SECTORS = 2


def contract_rows(left, right):
    return lax.dot_general(
        left, right, (((0,), (0,)), ((), ())), preferred_element_type=jnp.float32
    )


def exchange(x, distance, devices):
    return lax.ppermute(x, "row", [(i, i ^ distance) for i in range(devices)])


def halving_reduce_scatter(z, devices, order):
    bits = devices.bit_length() - 1
    me = lax.axis_index("row")
    cur = z.reshape((2,) * bits + (z.shape[0] // devices, z.shape[1]))
    left = list(range(bits - 1, -1, -1))
    for bit in order:
        axis = left.index(bit)
        left.remove(bit)
        mine = (me >> bit) & 1
        keep = lax.dynamic_index_in_dim(cur, mine, axis=axis, keepdims=False)
        send = lax.dynamic_index_in_dim(cur, 1 - mine, axis=axis, keepdims=False)
        cur = keep.astype(jnp.float32) + exchange(
            send.astype(jnp.bfloat16), 1 << bit, devices
        ).astype(jnp.float32)
    return cur


def doubling_all_gather(x, devices, order):
    me = lax.axis_index("row")
    cur = x
    done = []
    for bit in order:
        other = exchange(cur, 1 << bit, devices)
        low = (me >> bit) & 1 == 0
        axis = sum(1 for b in done if b > bit)
        done.append(bit)
        cur = jnp.stack(
            [jnp.where(low, cur, other), jnp.where(low, other, cur)], axis=axis
        )
    return cur.reshape((-1, x.shape[-1]))


def doubling_all_reduce(x, devices):
    bits = devices.bit_length() - 1
    low = 0
    while low < bits:
        width = 2 if low + 1 < bits else 1
        total = x
        for digit in range(1, 1 << width):
            total = total + exchange(x, digit << low, devices)
        x = total
        low += width
    return x


def stage_orders(devices):
    bits = list(range(devices.bit_length() - 1))
    if len(bits) < 3:
        return bits, bits
    return bits, [bits[0], bits[2], bits[1]] + bits[3:]


def shards(panels, first_f, first_g, phase, wavenum):
    chan_rows = first_f.shape[0]
    width = first_f.shape[1]
    devices = lax.axis_size("row")
    all_channels = chan_rows * devices
    first_row = lax.axis_index("row") * chan_rows
    order_amp, order_der = stage_orders(devices)
    gather_order_der = order_der[::-1]
    if len(gather_order_der) >= 4:
        gather_order_der = [gather_order_der[1], gather_order_der[0]] + gather_order_der[2:]
    amp_full = doubling_all_gather(first_f, devices, order_amp[::-1])
    der_full = doubling_all_gather(first_g, devices, gather_order_der)
    scale = None
    for sector in range(SECTORS):
        halves = []
        for gathered in (amp_full, der_full):
            projected = jnp.dot(panels[sector], gathered, preferred_element_type=jnp.float32)
            if scale is not None:
                projected = projected * scale[None, :]
            halves.append(
                contract_rows(panels[sector + 1], projected.astype(jnp.bfloat16)).astype(jnp.bfloat16)
            )
        rot_amp = halving_reduce_scatter(halves[0], devices, order_amp)
        rot_der = halving_reduce_scatter(halves[1], devices, order_der)
        angle_rows = lax.dynamic_slice_in_dim(phase[sector], first_row, chan_rows, 0)
        wave_rows = lax.dynamic_slice_in_dim(wavenum[sector], first_row, chan_rows, 0)
        cosine = jnp.cos(angle_rows)[:, None]
        sine = jnp.sin(angle_rows)[:, None]
        wave = wave_rows[:, None]
        new_amp = cosine * rot_amp + sine / wave * rot_der
        new_der = -wave * sine * rot_amp + cosine * rot_der
        if sector + 1 < SECTORS:
            amp_full = doubling_all_gather(new_amp.astype(jnp.bfloat16), devices, order_amp[::-1])
            der_full = doubling_all_gather(new_der.astype(jnp.bfloat16), devices, gather_order_der)
            amp_wide = amp_full.astype(jnp.float32)
            der_wide = der_full.astype(jnp.float32)
            norm = jnp.sum(amp_wide * amp_wide, axis=0) + jnp.sum(der_wide * der_wide, axis=0)
        else:
            local_norm = jnp.sum(new_amp * new_amp, axis=0) + jnp.sum(new_der * new_der, axis=0)
            norm = doubling_all_reduce(local_norm, devices)
        scale = 1.0 / jnp.sqrt(norm / (2.0 * all_channels) + 1e-06)
    return (new_amp * scale[None, :], new_der * scale[None, :])


def solution(mesh):
    in_specs = (
        P(None, "row", None),
        P("row", "grp"),
        P("row", "grp"),
        P("grp", None),
        P("grp", None),
    )
    out_specs = (P("row", "grp"), P("row", "grp"))
    return jax.shard_map(shards, mesh=mesh, in_specs=in_specs, out_specs=out_specs, check_vma=False)
```

```python
import jax
import jax.numpy as jnp
from jax import lax
from jax.sharding import PartitionSpec as P

SECTORS = 2


def contract_rows(left, right):
    return lax.dot_general(
        left, right, (((0,), (0,)), ((), ())), preferred_element_type=jnp.float32
    )


def exchange(x, distance, devices):
    return lax.ppermute(x, "row", [(i, i ^ distance) for i in range(devices)])


def halving_reduce_scatter(z, devices, order):
    bits = devices.bit_length() - 1
    me = lax.axis_index("row")
    cur = z.reshape((2,) * bits + (z.shape[0] // devices, z.shape[1]))
    left = list(range(bits - 1, -1, -1))
    for bit in order:
        axis = left.index(bit)
        left.remove(bit)
        mine = (me >> bit) & 1
        keep = lax.dynamic_index_in_dim(cur, mine, axis=axis, keepdims=False)
        send = lax.dynamic_index_in_dim(cur, 1 - mine, axis=axis, keepdims=False)
        cur = keep.astype(jnp.float32) + exchange(
            send.astype(jnp.bfloat16), 1 << bit, devices
        ).astype(jnp.float32)
    return cur


def doubling_all_gather(x, devices, order):
    me = lax.axis_index("row")
    cur = x
    done = []
    for bit in order:
        other = exchange(cur, 1 << bit, devices)
        low = (me >> bit) & 1 == 0
        axis = sum(1 for b in done if b > bit)
        done.append(bit)
        cur = jnp.stack(
            [jnp.where(low, cur, other), jnp.where(low, other, cur)], axis=axis
        )
    return cur.reshape((-1, x.shape[-1]))


def doubling_all_reduce(x, devices):
    bits = devices.bit_length() - 1
    low = 0
    while low < bits:
        width = 2 if low + 1 < bits else 1
        total = x
        for digit in range(1, 1 << width):
            total = total + exchange(x, digit << low, devices)
        x = total
        low += width
    return x


def stage_orders(devices):
    bits = list(range(devices.bit_length() - 1))
    if len(bits) < 3:
        return bits, bits
    return bits, [bits[0], bits[2], bits[1]] + bits[3:]


def shards(panels, first_f, first_g, phase, wavenum):
    chan_rows = first_f.shape[0]
    width = first_f.shape[1]
    devices = lax.axis_size("row")
    all_channels = chan_rows * devices
    first_row = lax.axis_index("row") * chan_rows
    order_amp, order_der = stage_orders(devices)
    amp_full = doubling_all_gather(first_f, devices, order_amp[::-1])
    der_full = doubling_all_gather(first_g, devices, order_der[::-1])
    scale = None
    for sector in range(SECTORS):
        halves = []
        for gathered in (amp_full, der_full):
            projected = jnp.dot(panels[sector], gathered, preferred_element_type=jnp.float32)
            halves.append(
                contract_rows(panels[sector + 1], projected.astype(jnp.bfloat16)).astype(jnp.bfloat16)
            )
        rot_amp = halving_reduce_scatter(halves[0], devices, order_amp)
        rot_der = halving_reduce_scatter(halves[1], devices, order_der)
        if scale is not None:
            rot_amp = rot_amp * scale[None, :]
            rot_der = rot_der * scale[None, :]
        angle_rows = lax.dynamic_slice_in_dim(phase[sector], first_row, chan_rows, 0)
        wave_rows = lax.dynamic_slice_in_dim(wavenum[sector], first_row, chan_rows, 0)
        cosine = jnp.cos(angle_rows)[:, None]
        sine = jnp.sin(angle_rows)[:, None]
        wave = wave_rows[:, None]
        new_amp = cosine * rot_amp + sine / wave * rot_der
        new_der = -wave * sine * rot_amp + cosine * rot_der
        if sector + 1 < SECTORS:
            amp_full = doubling_all_gather(new_amp.astype(jnp.bfloat16), devices, order_amp[::-1])
            der_full = doubling_all_gather(new_der.astype(jnp.bfloat16), devices, order_der[::-1])
            amp_wide = amp_full.astype(jnp.float32)
            der_wide = der_full.astype(jnp.float32)
            norm = jnp.sum(amp_wide * amp_wide, axis=0) + jnp.sum(der_wide * der_wide, axis=0)
        else:
            local_norm = jnp.sum(new_amp * new_amp, axis=0) + jnp.sum(new_der * new_der, axis=0)
            norm = doubling_all_reduce(local_norm, devices)
        scale = 1.0 / jnp.sqrt(norm / (2.0 * all_channels) + 1e-06)
    return (new_amp * scale[None, :], new_der * scale[None, :])


def solution(mesh):
    in_specs = (
        P(None, "row", None),
        P("row", "grp"),
        P("row", "grp"),
        P("grp", None),
        P("grp", None),
    )
    out_specs = (P("row", "grp"), P("row", "grp"))
    return jax.shard_map(shards, mesh=mesh, in_specs=in_specs, out_specs=out_specs, check_vma=False)
```

```python
import jax
import jax.numpy as jnp
from jax import lax
from jax.sharding import PartitionSpec as P

SECTORS = 2


def contract_rows(left, right):
    return lax.dot_general(
        left, right, (((0,), (0,)), ((), ())), preferred_element_type=jnp.float32
    )


def exchange(x, distance, devices):
    return lax.ppermute(x, "row", [(i, i ^ distance) for i in range(devices)])


def halving_reduce_scatter(z, devices, order, keep_pair=False):
    bits = devices.bit_length() - 1
    me = lax.axis_index("row")
    cur = z.reshape((2,) * bits + (z.shape[0] // devices, z.shape[1]))
    left = list(range(bits - 1, -1, -1))
    for bit in order:
        if keep_pair and bit == order[-1]:
            return cur.astype(jnp.float32) + exchange(
                cur.astype(jnp.bfloat16), 1 << bit, devices
            ).astype(jnp.float32)
        axis = left.index(bit)
        left.remove(bit)
        mine = (me >> bit) & 1
        keep = lax.dynamic_index_in_dim(cur, mine, axis=axis, keepdims=False)
        send = lax.dynamic_index_in_dim(cur, 1 - mine, axis=axis, keepdims=False)
        cur = keep.astype(jnp.float32) + exchange(
            send.astype(jnp.bfloat16), 1 << bit, devices
        ).astype(jnp.float32)
    return cur


def doubling_all_gather(x, devices, order, done=()):
    me = lax.axis_index("row")
    cur = x
    done = list(done)
    for bit in order:
        other = exchange(cur, 1 << bit, devices)
        low = (me >> bit) & 1 == 0
        axis = sum(1 for b in done if b > bit)
        done.append(bit)
        cur = jnp.stack(
            [jnp.where(low, cur, other), jnp.where(low, other, cur)], axis=axis
        )
    return cur.reshape((-1, x.shape[-1]))


def doubling_all_reduce(x, devices):
    bits = devices.bit_length() - 1
    low = 0
    while low < bits:
        width = 2 if low + 1 < bits else 1
        total = x
        for digit in range(1, 1 << width):
            total = total + exchange(x, digit << low, devices)
        x = total
        low += width
    return x


def stage_orders(devices):
    bits = list(range(devices.bit_length() - 1))
    if len(bits) < 3:
        return bits, bits
    return bits, [bits[0], bits[2], bits[1]] + bits[3:]


def shards(panels, first_f, first_g, phase, wavenum):
    chan_rows = first_f.shape[0]
    width = first_f.shape[1]
    devices = lax.axis_size("row")
    all_channels = chan_rows * devices
    first_row = lax.axis_index("row") * chan_rows
    order_amp, order_der = stage_orders(devices)
    amp_full = doubling_all_gather(first_f, devices, order_amp[::-1])
    der_full = doubling_all_gather(first_g, devices, order_der[::-1])
    scale = None
    for sector in range(SECTORS):
        halves = []
        for gathered in (amp_full, der_full):
            projected = jnp.dot(panels[sector], gathered, preferred_element_type=jnp.float32)
            if scale is not None:
                projected = projected * scale[None, :]
            halves.append(
                contract_rows(panels[sector + 1], projected.astype(jnp.bfloat16)).astype(jnp.bfloat16)
            )
        last = sector + 1 == SECTORS
        rot_amp = halving_reduce_scatter(halves[0], devices, order_amp, keep_pair=not last)
        rot_der = halving_reduce_scatter(halves[1], devices, order_der, keep_pair=not last)
        if last:
            blocks = [first_row]
        else:
            pair_bit = order_amp[-1]
            base = lax.axis_index("row") & ~(1 << pair_bit)
            blocks = [base * chan_rows, (base | (1 << pair_bit)) * chan_rows]
        angle_rows = jnp.stack(
            [lax.dynamic_slice_in_dim(phase[sector], b, chan_rows, 0) for b in blocks]
        ).reshape(rot_amp.shape[:-1] + (1,))
        wave_rows = jnp.stack(
            [lax.dynamic_slice_in_dim(wavenum[sector], b, chan_rows, 0) for b in blocks]
        ).reshape(rot_amp.shape[:-1] + (1,))
        cosine = jnp.cos(angle_rows)
        sine = jnp.sin(angle_rows)
        wave = wave_rows
        new_amp = cosine * rot_amp + sine / wave * rot_der
        new_der = -wave * sine * rot_amp + cosine * rot_der
        if sector + 1 < SECTORS:
            amp_full = doubling_all_gather(
                new_amp.astype(jnp.bfloat16), devices, order_amp[::-1][1:], done=order_amp[-1:]
            )
            der_full = doubling_all_gather(
                new_der.astype(jnp.bfloat16), devices, order_der[::-1][1:], done=order_der[-1:]
            )
            amp_wide = amp_full.astype(jnp.float32)
            der_wide = der_full.astype(jnp.float32)
            norm = jnp.sum(amp_wide * amp_wide, axis=0) + jnp.sum(der_wide * der_wide, axis=0)
        else:
            local_norm = jnp.sum(new_amp * new_amp, axis=0) + jnp.sum(new_der * new_der, axis=0)
            norm = doubling_all_reduce(local_norm, devices)
        scale = 1.0 / jnp.sqrt(norm / (2.0 * all_channels) + 1e-06)
    return (new_amp * scale[None, :], new_der * scale[None, :])


def solution(mesh):
    in_specs = (
        P(None, "row", None),
        P("row", "grp"),
        P("row", "grp"),
        P("grp", None),
        P("grp", None),
    )
    out_specs = (P("row", "grp"), P("row", "grp"))
    return jax.shard_map(shards, mesh=mesh, in_specs=in_specs, out_specs=out_specs, check_vma=False)
```

```python
import jax
import jax.numpy as jnp
from jax import lax
from jax.sharding import PartitionSpec as P

SECTORS = 2


def contract_rows(left, right):
    return lax.dot_general(
        left, right, (((0,), (0,)), ((), ())), preferred_element_type=jnp.float32
    )


def exchange(x, distance, devices):
    return lax.ppermute(x, "row", [(i, i ^ distance) for i in range(devices)])


def halving_reduce_scatter(z, devices, order, keep_pair=False):
    bits = devices.bit_length() - 1
    me = lax.axis_index("row")
    cur = z.reshape((2,) * bits + (z.shape[0] // devices, z.shape[1]))
    left = list(range(bits - 1, -1, -1))
    for bit in order:
        if keep_pair and bit == order[-1]:
            return cur.astype(jnp.float32) + exchange(
                cur.astype(jnp.bfloat16), 1 << bit, devices
            ).astype(jnp.float32)
        axis = left.index(bit)
        left.remove(bit)
        mine = (me >> bit) & 1
        keep = lax.dynamic_index_in_dim(cur, mine, axis=axis, keepdims=False)
        send = lax.dynamic_index_in_dim(cur, 1 - mine, axis=axis, keepdims=False)
        cur = keep.astype(jnp.float32) + exchange(
            send.astype(jnp.bfloat16), 1 << bit, devices
        ).astype(jnp.float32)
    return cur


def doubling_all_gather(x, devices, order, done=()):
    me = lax.axis_index("row")
    cur = x
    done = list(done)
    for bit in order:
        other = exchange(cur, 1 << bit, devices)
        low = (me >> bit) & 1 == 0
        axis = sum(1 for b in done if b > bit)
        done.append(bit)
        cur = jnp.stack(
            [jnp.where(low, cur, other), jnp.where(low, other, cur)], axis=axis
        )
    return cur.reshape((-1, x.shape[-1]))


def doubling_all_reduce(x, devices, bits=None):
    if bits is None:
        bits = devices.bit_length() - 1
    low = 0
    while low < bits:
        width = 2 if low + 1 < bits else 1
        total = x
        for digit in range(1, 1 << width):
            total = total + exchange(x, digit << low, devices)
        x = total
        low += width
    return x


def stage_orders(devices):
    bits = list(range(devices.bit_length() - 1))
    if len(bits) < 3:
        return bits, bits
    return bits, [bits[0], bits[2], bits[1]] + bits[3:]


def shards(panels, first_f, first_g, phase, wavenum):
    chan_rows = first_f.shape[0]
    width = first_f.shape[1]
    devices = lax.axis_size("row")
    all_channels = chan_rows * devices
    first_row = lax.axis_index("row") * chan_rows
    order_amp, order_der = stage_orders(devices)
    amp_full = doubling_all_gather(first_f, devices, order_amp[::-1])
    der_full = doubling_all_gather(first_g, devices, order_der[::-1])
    scale = None
    for sector in range(SECTORS):
        halves = []
        for gathered in (amp_full, der_full):
            projected = jnp.dot(panels[sector], gathered, preferred_element_type=jnp.float32)
            if scale is not None:
                projected = projected * scale[None, :]
            halves.append(
                contract_rows(panels[sector + 1], projected.astype(jnp.bfloat16)).astype(jnp.bfloat16)
            )
        last = sector + 1 == SECTORS
        rot_amp = halving_reduce_scatter(halves[0], devices, order_amp, keep_pair=True)
        rot_der = halving_reduce_scatter(halves[1], devices, order_der, keep_pair=True)
        pair_bit = order_amp[-1]
        base = lax.axis_index("row") & ~(1 << pair_bit)
        blocks = [base * chan_rows, (base | (1 << pair_bit)) * chan_rows]
        angle_rows = jnp.stack(
            [lax.dynamic_slice_in_dim(phase[sector], b, chan_rows, 0) for b in blocks]
        ).reshape(rot_amp.shape[:-1] + (1,))
        wave_rows = jnp.stack(
            [lax.dynamic_slice_in_dim(wavenum[sector], b, chan_rows, 0) for b in blocks]
        ).reshape(rot_amp.shape[:-1] + (1,))
        cosine = jnp.cos(angle_rows)
        sine = jnp.sin(angle_rows)
        wave = wave_rows
        new_amp = cosine * rot_amp + sine / wave * rot_der
        new_der = -wave * sine * rot_amp + cosine * rot_der
        if sector + 1 < SECTORS:
            amp_full = doubling_all_gather(
                new_amp.astype(jnp.bfloat16), devices, order_amp[::-1][1:], done=order_amp[-1:]
            )
            der_full = doubling_all_gather(
                new_der.astype(jnp.bfloat16), devices, order_der[::-1][1:], done=order_der[-1:]
            )
            amp_wide = amp_full.astype(jnp.float32)
            der_wide = der_full.astype(jnp.float32)
            norm = jnp.sum(amp_wide * amp_wide, axis=0) + jnp.sum(der_wide * der_wide, axis=0)
        else:
            local_norm = jnp.sum(new_amp * new_amp, axis=(0, 1)) + jnp.sum(new_der * new_der, axis=(0, 1))
            norm = doubling_all_reduce(local_norm, devices, bits=pair_bit)
            mine = (lax.axis_index("row") >> pair_bit) & 1
            new_amp = lax.dynamic_index_in_dim(new_amp, mine, axis=0, keepdims=False)
            new_der = lax.dynamic_index_in_dim(new_der, mine, axis=0, keepdims=False)
        scale = 1.0 / jnp.sqrt(norm / (2.0 * all_channels) + 1e-06)
    return (new_amp * scale[None, :], new_der * scale[None, :])


def solution(mesh):
    in_specs = (
        P(None, "row", None),
        P("row", "grp"),
        P("row", "grp"),
        P("grp", None),
        P("grp", None),
    )
    out_specs = (P("row", "grp"), P("row", "grp"))
    return jax.shard_map(shards, mesh=mesh, in_specs=in_specs, out_specs=out_specs, check_vma=False)
```
